128 devices in a mesh: blk: 8 (over z, y_hi), rep: 16 (over y_lo, x, core).
Axes of the slice: x: 4, y: 4 (y_hi: 2, y_lo: 2; y = y_hi * 2 + y_lo), z: 4, core: 2. Of those that a mesh axis runs over, the one named last changes fastest.
Arguments:
- photo_features: bfloat16 [16, 4096, 1152], P('rep', 'blk'), may hold values from -6 to 6
- wording_features: bfloat16 [16, 4096, 1152], P('rep', 'blk'), may hold values from -6 to 6
- partner_wording_slot: int32 [16, 4096], P('rep', 'blk'), may hold values from 0 to 4095, each once within a row
- photo_projector_weights: bfloat16 [1152, 1152], replicated, may hold values from -0.1875 to 0.1875
- wording_projector_weights: bfloat16 [1152, 1152], replicated, may hold values from -0.1875 to 0.1875
- learned_inverse_heat: float32 [1], replicated, may hold values from 4 to 12
- offset_term: float32 [1], replicated, may hold values from -3 to -1
Outputs:
- grad_img_head: float32 [1152, 1152], replicated
- grad_txt_head: float32 [1152, 1152], replicated
The draws below stay inside these ranges and needn't reach their ends.
Inputs may be any that keep to these rules, and one draw needn't show every extreme that they name: `partner_wording_slot`: within each group the 4096 images name distinct texts of that group.
All inputs are finite; a program needn't handle non-finite values.
Results may differ from the reference program's by a relative error of at most 0.0029.
Values may be sent and summed in bfloat16 or wider, within the bound.
No kernel may reach another device: no remote copies, remote signals or barrier semaphores. Data moves between devices by JAX's collectives and lax.ppermute only.
A program may use at most 128 MiB of HBM per device.

```python
import jax
import jax.numpy as jnp
from jax import lax

WIDTH = 1152
EMBED = 1152
ROWS_DEV = 512
STEPS = 4
GROUP_ROWS = 4096
N_BLK = 8
N_REP = 16


def block_scale(stream_key, shape, cuts, least, high):
    gain, own = 1.0, jax.random.fold_in(stream_key, 6)
    for axis_at, shards_of in cuts:
        heights = jnp.exp(jax.random.uniform(jax.random.fold_in(own, axis_at), (shards_of,), jnp.float32, least / len(cuts), high / len(cuts)))
        gain = gain * jnp.repeat(heights, shape[axis_at] // shards_of).reshape([-1 if axis == axis_at else 1 for axis in range(len(shape))])
    return gain


def centred(rng, extent, deviation, limit, pieces=(), kind=jnp.bfloat16):
    array = deviation * jax.random.normal(rng, extent, jnp.float32)
    if pieces:
        array = array * block_scale(rng, extent, pieces, -0.22, 0.18)
    return jnp.clip(array, -limit, limit).astype(kind)


def setup_inputs(seed: int = 0) -> dict:
    streams_of = jax.random.split(jax.random.key(seed), 8)
    return {
        "photo_features": centred(streams_of[0], (N_REP, GROUP_ROWS, WIDTH), 1.0, 6.0, ((0, 16), (1, 8))),
        "wording_features": centred(streams_of[1], (N_REP, GROUP_ROWS, WIDTH), 1.0, 6.0, ((0, 16), (1, 8))),
        "partner_wording_slot": jax.vmap(lambda own: jax.random.permutation(own, GROUP_ROWS))(jax.random.split(streams_of[2], N_REP)).reshape((N_REP, GROUP_ROWS)).astype(jnp.int32),
        "photo_projector_weights": centred(streams_of[3], (WIDTH, EMBED), WIDTH ** -0.5, 0.1875),
        "wording_projector_weights": centred(streams_of[4], (WIDTH, EMBED), WIDTH ** -0.5, 0.1875),
        "learned_inverse_heat": jnp.clip(jax.random.uniform(streams_of[5], (1,), jnp.float32, 4.0, 12.0), 4.0, 12.0),
        "offset_term": jnp.clip(jax.random.uniform(streams_of[6], (1,), jnp.float32, -3.0, -1.0), -3.0, -1.0),
    }


epsilon = 1e-06
criterion_prefactor = 0.0625

def normalize(features, head):
    projected = jnp.dot(features, head, preferred_element_type=jnp.float32)
    inverse = lax.rsqrt(lax.optimization_barrier(jnp.sum(projected * projected, axis=-1, keepdims=True)) + epsilon)
    unit = projected * inverse
    return (unit, unit.astype(jnp.bfloat16), inverse)

def unnormalize(unit, inverse, upstream):
    inner = lax.optimization_barrier(jnp.sum(unit * upstream, axis=-1, keepdims=True))
    return (inverse * (upstream - unit * inner)).astype(jnp.bfloat16)

def reference(photo_features, wording_features, partner_wording_slot, photo_projector_weights, wording_projector_weights, learned_inverse_heat, offset_term):
    positions = jnp.arange(GROUP_ROWS, dtype=jnp.int32)
    panel_of = positions // ROWS_DEV
    diagonal_band_span = (panel_of[:, None] - panel_of[None, :]) % N_BLK < STEPS
    exponentiated_heat = learned_inverse_heat[0] * criterion_prefactor

    def one_group(totals, group):
        image_rows, text_rows, targets = group
        img_unit, img_low, img_inv = normalize(image_rows, photo_projector_weights)
        txt_unit, txt_low, txt_inv = normalize(text_rows, wording_projector_weights)
        cosine_agreement_table = jnp.dot(img_low, txt_low.T, preferred_element_type=jnp.float32)
        unbounded_pairwise_array = learned_inverse_heat[0] * cosine_agreement_table + offset_term[0]
        diagonal_label = (targets[:, None] == positions[None, :]).astype(jnp.float32)
        sigmoid_error = jnp.where(diagonal_band_span, exponentiated_heat * (jax.nn.sigmoid(unbounded_pairwise_array) - diagonal_label), 0.0).astype(jnp.bfloat16)
        d_img = jnp.dot(sigmoid_error, txt_low, preferred_element_type=jnp.float32)
        d_txt = jnp.dot(sigmoid_error.T, img_low, preferred_element_type=jnp.float32)
        grad_img = jnp.dot(image_rows.T, unnormalize(img_unit, img_inv, d_img), preferred_element_type=jnp.float32)
        grad_txt = jnp.dot(text_rows.T, unnormalize(txt_unit, txt_inv, d_txt), preferred_element_type=jnp.float32)
        return ((totals[0] + grad_img, totals[1] + grad_txt), None)
    zeros = jnp.zeros((WIDTH, EMBED), jnp.float32)
    totals, unused = lax.scan(one_group, (zeros, zeros), (photo_features, wording_features, partner_wording_slot))
    return (totals[0], totals[1])
```

```python
import jax
import jax.numpy as jnp
from jax import lax
from jax.sharding import PartitionSpec as P

STEPS = 4


epsilon = 1e-06
criterion_prefactor = 0.0625


def shifted(array, axis, by):
    count = lax.axis_size(axis)
    return lax.ppermute(array, axis, [(i, (i + by) % count) for i in range(count)])


def normalize(features, head):
    projected = jnp.dot(features, head, preferred_element_type=jnp.float32)
    inverse = lax.rsqrt(jnp.sum(projected * projected, axis=-1, keepdims=True) + epsilon)
    unit = projected * inverse
    return (unit, unit.astype(jnp.bfloat16), inverse)


def unnormalize(unit, inverse, upstream):
    inner = jnp.sum(unit * upstream, axis=-1, keepdims=True)
    return (inverse * (upstream - unit * inner)).astype(jnp.bfloat16)


def residual(img, txt, targets, first_column, heat, offset):
    table = lax.dot_general(img, txt, (((1,), (1,)), ((), ())), preferred_element_type=jnp.float32)
    logits = heat * table + offset
    columns = first_column + jnp.arange(txt.shape[0], dtype=jnp.int32)
    label = (targets[:, None] == columns[None, :]).astype(jnp.float32)
    return (heat * criterion_prefactor * (jax.nn.sigmoid(logits) - label)).astype(jnp.bfloat16)


def head_grad_t(features, du):
    return lax.dot_general(du, features, (((0,), (0,)), ((), ())), preferred_element_type=jnp.float32)


def local(
    photo_features,
    wording_features,
    partner_wording_slot,
    photo_projector_weights,
    wording_projector_weights,
    learned_inverse_heat,
    offset_term,
):
    image_rows = photo_features[0]
    text_rows = wording_features[0]
    targets = partner_wording_slot[0]
    rows = image_rows.shape[0]
    blocks = lax.axis_size("blk")
    me = lax.axis_index("blk")
    heat = learned_inverse_heat[0]
    offset = offset_term[0]
    img_unit, img_low, img_inv = normalize(image_rows, photo_projector_weights)
    txt_unit, txt_low, txt_inv = normalize(text_rows, wording_projector_weights)

    txt_from = [txt_low] + [shifted(txt_low, "blk", d) for d in range(1, STEPS)]
    img_from = [img_low] + [shifted(img_low, "blk", -d) for d in range(1, STEPS)]
    tgt_from = [targets] + [shifted(targets, "blk", -d) for d in range(1, STEPS)]

    own_first = me * rows
    diagonal = residual(img_low, txt_low, targets, own_first, heat, offset)
    d_img = jnp.dot(diagonal, txt_low, preferred_element_type=jnp.float32)
    d_txt = lax.dot_general(diagonal, img_low, (((0,), (0,)), ((), ())), preferred_element_type=jnp.float32)
    for d in range(1, STEPS):
        first = (me - d) % blocks * rows
        piece = residual(img_low, txt_from[d], targets, first, heat, offset)
        d_img = d_img + jnp.dot(piece, txt_from[d], preferred_element_type=jnp.float32)
        piece = residual(img_from[d], txt_low, tgt_from[d], own_first, heat, offset)
        d_txt = d_txt + lax.dot_general(
            piece, img_from[d], (((0,), (0,)), ((), ())), preferred_element_type=jnp.float32
        )
    grad_img = head_grad_t(image_rows, unnormalize(img_unit, img_inv, d_img))
    grad_txt = head_grad_t(text_rows, unnormalize(txt_unit, txt_inv, d_txt))
    grad_img, grad_txt = lax.psum((grad_img, grad_txt), ("blk", "rep"))
    return (grad_img.T, grad_txt.T)


def solution(mesh):
    placed = (P("rep", "blk", None), P("rep", "blk", None), P("rep", "blk"), P(), P(), P(), P())
    return jax.shard_map(local, mesh=mesh, in_specs=placed, out_specs=(P(), P()), check_vma=False)
```

```python
import jax
import jax.numpy as jnp
from jax import lax
from jax.sharding import PartitionSpec as P
from jax.experimental.layout import Layout, with_layout_constraint

STEPS = 4


epsilon = 1e-06
criterion_prefactor = 0.0625


def shifted(array, axis, by):
    count = lax.axis_size(axis)
    return lax.ppermute(array, axis, [(i, (i + by) % count) for i in range(count)])


def normalize(features, head):
    projected = jnp.dot(features, head, preferred_element_type=jnp.float32)
    inverse = lax.rsqrt(jnp.sum(projected * projected, axis=-1, keepdims=True) + epsilon)
    unit = projected * inverse
    return (unit, unit.astype(jnp.bfloat16), inverse)


def unnormalize(unit, inverse, upstream):
    inner = jnp.sum(unit * upstream, axis=-1, keepdims=True)
    return (inverse * (upstream - unit * inner)).astype(jnp.bfloat16)


def residual(img, txt, targets, first_column, heat, offset):
    table = lax.dot_general(img, txt, (((1,), (1,)), ((), ())), preferred_element_type=jnp.float32)
    logits = heat * table + offset
    columns = first_column + jnp.arange(txt.shape[0], dtype=jnp.int32)
    label = (targets[:, None] == columns[None, :]).astype(jnp.float32)
    return (heat * criterion_prefactor * (jax.nn.sigmoid(logits) - label)).astype(jnp.bfloat16)


def head_grad_t(features, du):
    return lax.dot_general(du, features, (((0,), (0,)), ((), ())), preferred_element_type=jnp.float32)


def local(
    photo_features,
    wording_features,
    partner_wording_slot,
    photo_projector_weights,
    wording_projector_weights,
    learned_inverse_heat,
    offset_term,
):
    image_rows = photo_features[0]
    text_rows = wording_features[0]
    targets = partner_wording_slot[0]
    rows = image_rows.shape[0]
    blocks = lax.axis_size("blk")
    me = lax.axis_index("blk")
    heat = learned_inverse_heat[0]
    offset = offset_term[0]
    text_from = [shifted(text_rows, "blk", d) for d in range(STEPS - 1, 0, -1)][::-1]
    image_from = [shifted(image_rows, "blk", -d) for d in range(STEPS - 1, 0, -1)][::-1]
    tgt_from = [targets] + [shifted(targets, "blk", -d) for d in range(1, STEPS)]
    img_unit, img_low, img_inv = normalize(image_rows, photo_projector_weights)
    txt_unit, txt_low, txt_inv = normalize(text_rows, wording_projector_weights)
    txt_from = [txt_low] + [normalize(rows_in, wording_projector_weights)[1] for rows_in in text_from]
    img_from = [img_low] + [normalize(rows_in, photo_projector_weights)[1] for rows_in in image_from]

    own_first = me * rows
    diagonal = residual(img_low, txt_low, targets, own_first, heat, offset)
    d_img = jnp.dot(diagonal, txt_low, preferred_element_type=jnp.float32)
    d_txt = lax.dot_general(diagonal, img_low, (((0,), (0,)), ((), ())), preferred_element_type=jnp.float32)
    for d in range(1, STEPS):
        first = (me - d) % blocks * rows
        piece = residual(img_low, txt_from[d], targets, first, heat, offset)
        d_img = d_img + jnp.dot(piece, txt_from[d], preferred_element_type=jnp.float32)
        piece = residual(img_from[d], txt_low, tgt_from[d], own_first, heat, offset)
        d_txt = d_txt + lax.dot_general(
            piece, img_from[d], (((0,), (0,)), ((), ())), preferred_element_type=jnp.float32
        )
    grad_img = head_grad_t(image_rows, unnormalize(img_unit, img_inv, d_img))
    grad_txt = head_grad_t(text_rows, unnormalize(txt_unit, txt_inv, d_txt))
    row_major = (Layout((0, 1)), Layout((0, 1)))
    grad_img, grad_txt = with_layout_constraint((grad_img.T, grad_txt.T), row_major)
    return lax.psum((grad_img, grad_txt), ("blk", "rep"))


def solution(mesh):
    placed = (P("rep", "blk", None), P("rep", "blk", None), P("rep", "blk"), P(), P(), P(), P())
    return jax.shard_map(local, mesh=mesh, in_specs=placed, out_specs=(P(), P()), check_vma=False)
```

```python
import jax
import jax.numpy as jnp
from jax import lax
from jax.sharding import PartitionSpec as P
from jax.experimental.layout import Layout, with_layout_constraint

STEPS = 4


epsilon = 1e-06
criterion_prefactor = 0.0625


def shifted(array, axis, by):
    count = lax.axis_size(axis)
    return lax.ppermute(array, axis, [(i, (i + by) % count) for i in range(count)])


def normalize(features, head):
    projected = jnp.dot(features, head, preferred_element_type=jnp.float32)
    inverse = lax.rsqrt(jnp.sum(projected * projected, axis=-1, keepdims=True) + epsilon)
    unit = projected * inverse
    return (unit, unit.astype(jnp.bfloat16), inverse)


def unnormalize(unit, inverse, upstream):
    inner = jnp.sum(unit * upstream, axis=-1, keepdims=True)
    return (inverse * (upstream - unit * inner)).astype(jnp.bfloat16)


def residual(img, txt, targets, first_column, heat, offset):
    table = lax.dot_general(img, txt, (((1,), (1,)), ((), ())), preferred_element_type=jnp.float32)
    logits = heat * table + offset
    columns = first_column + jnp.arange(txt.shape[0], dtype=jnp.int32)
    label = (targets[:, None] == columns[None, :]).astype(jnp.float32)
    return (heat * criterion_prefactor * (jax.nn.sigmoid(logits) - label)).astype(jnp.bfloat16)


def head_grad_t(features, du):
    return lax.dot_general(du, features, (((0,), (0,)), ((), ())), preferred_element_type=jnp.float32)


def local(
    photo_features,
    wording_features,
    partner_wording_slot,
    photo_projector_weights,
    wording_projector_weights,
    learned_inverse_heat,
    offset_term,
):
    image_rows = photo_features[0]
    text_rows = wording_features[0]
    targets = partner_wording_slot[0]
    rows = image_rows.shape[0]
    blocks = lax.axis_size("blk")
    me = lax.axis_index("blk")
    heat = learned_inverse_heat[0]
    offset = offset_term[0]
    img_unit, img_low, img_inv = normalize(image_rows, photo_projector_weights)
    txt_unit, txt_low, txt_inv = normalize(text_rows, wording_projector_weights)

    txt_from = [txt_low] + [shifted(txt_low, "blk", d) for d in range(1, STEPS)]
    img_from = [img_low] + [shifted(img_low, "blk", -d) for d in range(1, STEPS)]
    tgt_from = [targets] + [shifted(targets, "blk", -d) for d in range(1, STEPS)]

    own_first = me * rows
    diagonal = residual(img_low, txt_low, targets, own_first, heat, offset)
    d_img = jnp.dot(diagonal, txt_low, preferred_element_type=jnp.float32)
    d_txt = lax.dot_general(diagonal, img_low, (((0,), (0,)), ((), ())), preferred_element_type=jnp.float32)
    for d in range(1, STEPS):
        first = (me - d) % blocks * rows
        piece = residual(img_low, txt_from[d], targets, first, heat, offset)
        d_img = d_img + jnp.dot(piece, txt_from[d], preferred_element_type=jnp.float32)
        piece = residual(img_from[d], txt_low, tgt_from[d], own_first, heat, offset)
        d_txt = d_txt + lax.dot_general(
            piece, img_from[d], (((0,), (0,)), ((), ())), preferred_element_type=jnp.float32
        )
    grad_img = head_grad_t(image_rows, unnormalize(img_unit, img_inv, d_img))
    grad_txt = head_grad_t(text_rows, unnormalize(txt_unit, txt_inv, d_txt))
    row_major = (Layout((0, 1)), Layout((0, 1)))
    grad_img, grad_txt = with_layout_constraint((grad_img.T, grad_txt.T), row_major)
    return lax.psum((grad_img, grad_txt), ("blk", "rep"))


def solution(mesh):
    placed = (P("rep", "blk", None), P("rep", "blk", None), P("rep", "blk"), P(), P(), P(), P())
    return jax.shard_map(local, mesh=mesh, in_specs=placed, out_specs=(P(), P()), check_vma=False)
```

```python
import jax
import jax.numpy as jnp
from jax import lax
from jax.sharding import PartitionSpec as P
from jax.experimental.layout import Layout, with_layout_constraint

STEPS = 4


epsilon = 1e-06
criterion_prefactor = 0.0625


def shifted(array, axis, by):
    count = lax.axis_size(axis)
    return lax.ppermute(array, axis, [(i, (i + by) % count) for i in range(count)])


def normalize(features, head):
    projected = jnp.dot(features, head, preferred_element_type=jnp.float32)
    inverse = lax.rsqrt(jnp.sum(projected * projected, axis=-1, keepdims=True) + epsilon)
    unit = projected * inverse
    return (unit, unit.astype(jnp.bfloat16), inverse)


def unnormalize(unit, inverse, upstream):
    inner = jnp.sum(unit * upstream, axis=-1, keepdims=True)
    return (inverse * (upstream - unit * inner)).astype(jnp.bfloat16)


def residual(img, txt, targets, first_column, heat, offset):
    table = lax.dot_general(img, txt, (((1,), (1,)), ((), ())), preferred_element_type=jnp.float32)
    logits = heat * table + offset
    columns = first_column + jnp.arange(txt.shape[0], dtype=jnp.int32)
    label = (targets[:, None] == columns[None, :]).astype(jnp.float32)
    return (heat * criterion_prefactor * (jax.nn.sigmoid(logits) - label)).astype(jnp.bfloat16)


def head_grad_t(features, du):
    return lax.dot_general(du, features, (((0,), (0,)), ((), ())), preferred_element_type=jnp.float32)


def local(
    photo_features,
    wording_features,
    partner_wording_slot,
    photo_projector_weights,
    wording_projector_weights,
    learned_inverse_heat,
    offset_term,
):
    image_rows = photo_features[0]
    text_rows = wording_features[0]
    targets = partner_wording_slot[0]
    rows = image_rows.shape[0]
    blocks = lax.axis_size("blk")
    me = lax.axis_index("blk")
    heat = learned_inverse_heat[0]
    offset = offset_term[0]
    img_unit, img_low, img_inv = normalize(image_rows, photo_projector_weights)
    txt_unit, txt_low, txt_inv = normalize(text_rows, wording_projector_weights)
    img_low, txt_low = lax.optimization_barrier((img_low, txt_low))

    txt_from = [txt_low] + [shifted(txt_low, "blk", d) for d in range(1, STEPS)]
    img_from = [img_low] + [shifted(img_low, "blk", -d) for d in range(1, STEPS)]
    tgt_from = [targets] + [shifted(targets, "blk", -d) for d in range(1, STEPS)]

    own_first = me * rows
    diagonal = residual(img_low, txt_low, targets, own_first, heat, offset)
    d_img = jnp.dot(diagonal, txt_low, preferred_element_type=jnp.float32)
    d_txt = lax.dot_general(diagonal, img_low, (((0,), (0,)), ((), ())), preferred_element_type=jnp.float32)
    for d in range(1, STEPS):
        first = (me - d) % blocks * rows
        piece = residual(img_low, txt_from[d], targets, first, heat, offset)
        d_img = d_img + jnp.dot(piece, txt_from[d], preferred_element_type=jnp.float32)
        piece = residual(img_from[d], txt_low, tgt_from[d], own_first, heat, offset)
        d_txt = d_txt + lax.dot_general(
            piece, img_from[d], (((0,), (0,)), ((), ())), preferred_element_type=jnp.float32
        )
    grad_img = head_grad_t(image_rows, unnormalize(img_unit, img_inv, d_img))
    grad_txt = head_grad_t(text_rows, unnormalize(txt_unit, txt_inv, d_txt))
    row_major = (Layout((0, 1)), Layout((0, 1)))
    grad_img, grad_txt = with_layout_constraint((grad_img.T, grad_txt.T), row_major)
    return lax.psum((grad_img, grad_txt), ("blk", "rep"))


def solution(mesh):
    placed = (P("rep", "blk", None), P("rep", "blk", None), P("rep", "blk"), P(), P(), P(), P())
    return jax.shard_map(local, mesh=mesh, in_specs=placed, out_specs=(P(), P()), check_vma=False)
```

```python
import jax
import jax.numpy as jnp
from jax import lax
from jax.sharding import PartitionSpec as P
from jax.experimental.layout import Layout, with_layout_constraint

STEPS = 4


epsilon = 1e-06
criterion_prefactor = 0.0625


def shifted(array, axis, by):
    count = lax.axis_size(axis)
    return lax.ppermute(array, axis, [(i, (i + by) % count) for i in range(count)])


def normalize(features, head):
    projected = jnp.dot(features, head, preferred_element_type=jnp.float32)
    inverse = lax.rsqrt(jnp.sum(projected * projected, axis=-1, keepdims=True) + epsilon)
    unit = projected * inverse
    return (unit, unit.astype(jnp.bfloat16), inverse)


def unnormalize(unit, inverse, upstream):
    inner = jnp.sum(unit * upstream, axis=-1, keepdims=True)
    return (inverse * (upstream - unit * inner)).astype(jnp.bfloat16)


def residual(img, txt, targets, first_column, heat, offset):
    table = lax.dot_general(img, txt, (((1,), (1,)), ((), ())), preferred_element_type=jnp.float32)
    logits = heat * table + offset
    columns = first_column + jnp.arange(txt.shape[0], dtype=jnp.int32)
    label = (targets[:, None] == columns[None, :]).astype(jnp.float32)
    return (heat * criterion_prefactor * (jax.nn.sigmoid(logits) - label)).astype(jnp.bfloat16)


def head_grad_t(features, du):
    return lax.dot_general(du, features, (((0,), (0,)), ((), ())), preferred_element_type=jnp.float32)


def local(
    photo_features,
    wording_features,
    partner_wording_slot,
    photo_projector_weights,
    wording_projector_weights,
    learned_inverse_heat,
    offset_term,
):
    image_rows = photo_features[0]
    text_rows = wording_features[0]
    targets = partner_wording_slot[0]
    rows = image_rows.shape[0]
    blocks = lax.axis_size("blk")
    me = lax.axis_index("blk")
    heat = learned_inverse_heat[0]
    offset = offset_term[0]
    img_unit, img_low, img_inv = normalize(image_rows, photo_projector_weights)
    txt_unit, txt_low, txt_inv = normalize(text_rows, wording_projector_weights)

    txt_from = [txt_low] + [shifted(txt_low, "blk", d) for d in range(1, STEPS)]
    width = img_low.shape[1]
    digits = jnp.concatenate([targets // 64, targets % 64]).astype(jnp.bfloat16)
    code_row = jnp.zeros((1, width), jnp.bfloat16).at[0, : 2 * rows].set(digits)
    img_coded = jnp.concatenate([img_low, code_row], 0)
    img_from, tgt_from = [img_low], [targets]
    for d in range(1, STEPS):
        arrived = shifted(img_coded, "blk", -d)
        code = arrived[rows].astype(jnp.int32)
        img_from.append(arrived[:rows])
        tgt_from.append(code[:rows] * 64 + code[rows : 2 * rows])

    own_first = me * rows
    diagonal = residual(img_low, txt_low, targets, own_first, heat, offset)
    d_img = jnp.dot(diagonal, txt_low, preferred_element_type=jnp.float32)
    d_txt = lax.dot_general(diagonal, img_low, (((0,), (0,)), ((), ())), preferred_element_type=jnp.float32)
    for d in range(1, STEPS):
        first = (me - d) % blocks * rows
        piece = residual(img_low, txt_from[d], targets, first, heat, offset)
        d_img = d_img + jnp.dot(piece, txt_from[d], preferred_element_type=jnp.float32)
        piece = residual(img_from[d], txt_low, tgt_from[d], own_first, heat, offset)
        d_txt = d_txt + lax.dot_general(
            piece, img_from[d], (((0,), (0,)), ((), ())), preferred_element_type=jnp.float32
        )
    grad_img = head_grad_t(image_rows, unnormalize(img_unit, img_inv, d_img))
    grad_txt = head_grad_t(text_rows, unnormalize(txt_unit, txt_inv, d_txt))
    row_major = (Layout((0, 1)), Layout((0, 1)))
    grad_img, grad_txt = with_layout_constraint((grad_img.T, grad_txt.T), row_major)
    return lax.psum((grad_img, grad_txt), ("blk", "rep"))


def solution(mesh):
    placed = (P("rep", "blk", None), P("rep", "blk", None), P("rep", "blk"), P(), P(), P(), P())
    return jax.shard_map(local, mesh=mesh, in_specs=placed, out_specs=(P(), P()), check_vma=False)
```

```python
import jax
import jax.numpy as jnp
from jax import lax
from jax.sharding import PartitionSpec as P
from jax.experimental.layout import Layout, with_layout_constraint

STEPS = 4


epsilon = 1e-06
criterion_prefactor = 0.0625


def shifted(array, axis, by):
    count = lax.axis_size(axis)
    return lax.ppermute(array, axis, [(i, (i + by) % count) for i in range(count)])


def normalize(features, head):
    projected = jnp.dot(features, head, preferred_element_type=jnp.float32)
    inverse = lax.rsqrt(jnp.sum(projected * projected, axis=-1, keepdims=True) + epsilon)
    unit = projected * inverse
    return (unit, unit.astype(jnp.bfloat16), inverse)


def unnormalize(unit, inverse, upstream):
    inner = jnp.sum(unit * upstream, axis=-1, keepdims=True)
    return (inverse * (upstream - unit * inner)).astype(jnp.bfloat16)


def residual(img, txt, targets, first_column, heat, offset):
    table = lax.dot_general(img, txt, (((1,), (1,)), ((), ())), preferred_element_type=jnp.float32)
    logits = heat * table + offset
    columns = first_column + jnp.arange(txt.shape[0], dtype=jnp.int32)
    label = (targets[:, None] == columns[None, :]).astype(jnp.float32)
    return (heat * criterion_prefactor * (jax.nn.sigmoid(logits) - label)).astype(jnp.bfloat16)


def head_grad_t(features, du):
    return lax.dot_general(du, features, (((0,), (0,)), ((), ())), preferred_element_type=jnp.float32)


def local(
    photo_features,
    wording_features,
    partner_wording_slot,
    photo_projector_weights,
    wording_projector_weights,
    learned_inverse_heat,
    offset_term,
):
    image_rows = photo_features[0]
    text_rows = wording_features[0]
    targets = partner_wording_slot[0]
    rows = image_rows.shape[0]
    blocks = lax.axis_size("blk")
    me = lax.axis_index("blk")
    heat = learned_inverse_heat[0]
    offset = offset_term[0]
    img_unit, img_low, img_inv = normalize(image_rows, photo_projector_weights)
    txt_unit, txt_low, txt_inv = normalize(text_rows, wording_projector_weights)

    half = rows // 2
    halves = [slice(0, half), slice(half, rows)]
    txt_from = [[shifted(txt_low[h], "blk", d) for h in halves] for d in range(1, STEPS)]
    img_from = [[shifted(img_low[h], "blk", -d) for h in halves] for d in range(1, STEPS)]
    tgt_from = [shifted(targets, "blk", -d) for d in range(1, STEPS)]

    own_first = me * rows
    diagonal = residual(img_low, txt_low, targets, own_first, heat, offset)
    d_img = jnp.dot(diagonal, txt_low, preferred_element_type=jnp.float32)
    d_txt = lax.dot_general(diagonal, img_low, (((0,), (0,)), ((), ())), preferred_element_type=jnp.float32)
    for d in range(1, STEPS):
        first = (me - d) % blocks * rows
        for k, h in enumerate(halves):
            txt_part = txt_from[d - 1][k]
            piece = residual(img_low, txt_part, targets, first + k * half, heat, offset)
            d_img = d_img + jnp.dot(piece, txt_part, preferred_element_type=jnp.float32)
            img_part = img_from[d - 1][k]
            piece = residual(img_part, txt_low, tgt_from[d - 1][h], own_first, heat, offset)
            d_txt = d_txt + lax.dot_general(
                piece, img_part, (((0,), (0,)), ((), ())), preferred_element_type=jnp.float32
            )
    grad_img = head_grad_t(image_rows, unnormalize(img_unit, img_inv, d_img))
    grad_txt = head_grad_t(text_rows, unnormalize(txt_unit, txt_inv, d_txt))
    row_major = (Layout((0, 1)), Layout((0, 1)))
    grad_img, grad_txt = with_layout_constraint((grad_img.T, grad_txt.T), row_major)
    return lax.psum((grad_img, grad_txt), ("blk", "rep"))


def solution(mesh):
    placed = (P("rep", "blk", None), P("rep", "blk", None), P("rep", "blk"), P(), P(), P(), P())
    return jax.shard_map(local, mesh=mesh, in_specs=placed, out_specs=(P(), P()), check_vma=False)
```

```python
import jax
import jax.numpy as jnp
from jax import lax
from jax.sharding import PartitionSpec as P
from jax.experimental.layout import Layout, with_layout_constraint

STEPS = 4


epsilon = 1e-06
criterion_prefactor = 0.0625


def shifted(array, axis, by):
    count = lax.axis_size(axis)
    return lax.ppermute(array, axis, [(i, (i + by) % count) for i in range(count)])


def normalize(features, head):
    projected = jnp.dot(features, head, preferred_element_type=jnp.float32)
    inverse = lax.rsqrt(jnp.sum(projected * projected, axis=-1, keepdims=True) + epsilon)
    unit = projected * inverse
    return (unit, unit.astype(jnp.bfloat16), inverse)


def unnormalize(unit, inverse, upstream):
    products = (unit * upstream).reshape(unit.shape[0], -1, 128)
    partial = lax.optimization_barrier(jnp.sum(products, axis=-1))
    inner = jnp.sum(partial, axis=-1, keepdims=True)
    return (inverse * (upstream - unit * inner)).astype(jnp.bfloat16)


def residual(img, txt, targets, first_column, heat, offset):
    table = lax.dot_general(img, txt, (((1,), (1,)), ((), ())), preferred_element_type=jnp.float32)
    logits = heat * table + offset
    columns = first_column + jnp.arange(txt.shape[0], dtype=jnp.int32)
    label = (targets[:, None] == columns[None, :]).astype(jnp.float32)
    return (heat * criterion_prefactor * (jax.nn.sigmoid(logits) - label)).astype(jnp.bfloat16)


def head_grad_t(features, du):
    return lax.dot_general(du, features, (((0,), (0,)), ((), ())), preferred_element_type=jnp.float32)


def local(
    photo_features,
    wording_features,
    partner_wording_slot,
    photo_projector_weights,
    wording_projector_weights,
    learned_inverse_heat,
    offset_term,
):
    image_rows = photo_features[0]
    text_rows = wording_features[0]
    targets = partner_wording_slot[0]
    rows = image_rows.shape[0]
    blocks = lax.axis_size("blk")
    me = lax.axis_index("blk")
    heat = learned_inverse_heat[0]
    offset = offset_term[0]
    img_unit, img_low, img_inv = normalize(image_rows, photo_projector_weights)
    txt_unit, txt_low, txt_inv = normalize(text_rows, wording_projector_weights)

    txt_from = [txt_low] + [shifted(txt_low, "blk", d) for d in range(1, STEPS)]
    img_from = [img_low] + [shifted(img_low, "blk", -d) for d in range(1, STEPS)]
    tgt_from = [targets] + [shifted(targets, "blk", -d) for d in range(1, STEPS)]

    own_first = me * rows
    diagonal = residual(img_low, txt_low, targets, own_first, heat, offset)
    d_img = jnp.dot(diagonal, txt_low, preferred_element_type=jnp.float32)
    d_txt = lax.dot_general(diagonal, img_low, (((0,), (0,)), ((), ())), preferred_element_type=jnp.float32)
    for d in range(1, STEPS):
        first = (me - d) % blocks * rows
        piece = residual(img_low, txt_from[d], targets, first, heat, offset)
        d_img = d_img + jnp.dot(piece, txt_from[d], preferred_element_type=jnp.float32)
        piece = residual(img_from[d], txt_low, tgt_from[d], own_first, heat, offset)
        d_txt = d_txt + lax.dot_general(
            piece, img_from[d], (((0,), (0,)), ((), ())), preferred_element_type=jnp.float32
        )
    grad_img = head_grad_t(image_rows, unnormalize(img_unit, img_inv, d_img))
    grad_txt = head_grad_t(text_rows, unnormalize(txt_unit, txt_inv, d_txt))
    row_major = (Layout((0, 1)), Layout((0, 1)))
    grad_img, grad_txt = with_layout_constraint((grad_img.T, grad_txt.T), row_major)
    return lax.psum((grad_img, grad_txt), ("blk", "rep"))


def solution(mesh):
    placed = (P("rep", "blk", None), P("rep", "blk", None), P("rep", "blk"), P(), P(), P(), P())
    return jax.shard_map(local, mesh=mesh, in_specs=placed, out_specs=(P(), P()), check_vma=False)
```
